32 devices in a mesh: ax: 2 (over y), az: 16 (over z, x, core).
Axes of the slice: x: 2, y: 2, z: 4, core: 2. Of those that a mesh axis runs over, the one named last changes fastest.
Arguments:
- state: float32 [4, 64, 128, 128], P(None, 'ax', 'az'), may hold values from -6 to 6
- final_adjoint: float32 [4, 64, 128, 128], P(None, 'ax', 'az'), may hold values from -6 to 6
- resistance: float32 [512], replicated, may hold values from 0.2 to 2
- wall_patch: int32 [64, 128], P('ax', 'az'), may hold values from 0 to 511
- patch_slot_index: int32 [512], replicated, may hold values from 0 to 1023, as said below
Outputs:
- initial_adjoint: float32 [4, 64, 128, 128], P(None, 'ax', 'az')
- patch_gradient: float32 [1024], P('az')
The draws below stay inside these ranges and needn't reach their ends.
Inputs may be any that keep to these rules, and one draw needn't show every extreme that they name: `patch_slot_index`: the values are distinct; 0 and 1023 are always among them.
All inputs are finite; a program needn't handle non-finite values.
Results may differ from the reference program's by a relative error of at most 0.0003.
Values sent between devices are 32-bit elements; how exact they have to be, the bound alone decides.
No kernel may reach another device: no remote copies, remote signals or barrier semaphores. Data moves between devices by JAX's collectives and lax.ppermute only.
A program may use at most 128 MiB of HBM per device.

```python
import math
import jax
import jax.numpy as jnp
import numpy as np

CR = 128
ITERS = 4
NA = 64
NT = 128
TOTAL_SLOT_COUNT = 1024
PATCHES = 512


def draw_patch_slot_index(key, part):
    halved_count = TOTAL_SLOT_COUNT // 2
    coins = jax.random.randint(jax.random.fold_in(key, 11), (halved_count,), 0, 2)
    coins = coins.at[0].set(0).at[halved_count - 1].set(1)
    chosen = jnp.arange(halved_count, dtype=jnp.int32) + coins * halved_count
    order = jax.random.permutation(jax.random.fold_in(key, 12), halved_count)
    return chosen[order].astype(jnp.int32)


def set_ends(values, stream_key, least, largest):
    longest = values.shape.index(max(values.shape))
    spots = []
    for shift in (0, 1):
        where = [jax.random.randint(jax.random.fold_in(stream_key, axis), (), 0, length) for axis, length in enumerate(values.shape)]
        where[longest] = (where[longest] + shift) % values.shape[longest]
        spots.append(tuple(where))
    return values.at[spots[0]].set(least).at[spots[1]].set(largest)


def shard_levels(key, dims, pieces, smallest, top_value):
    def one(dim, parts):
        draws = jax.random.uniform(jax.random.fold_in(jax.random.fold_in(key, 6), dim), (parts,), jnp.float32, smallest / len(pieces), top_value / len(pieces))
        return jnp.repeat(jnp.exp(draws), dims[dim] // parts).reshape((-1,) + (1,) * (len(dims) - dim - 1))

    gain = one(*pieces[0])
    for cut in pieces[1:]:
        gain = gain * one(*cut)
    return gain


def cumulative_ranks(count, slope):
    weights = [(1 << 20) // math.isqrt(rank ** slope) + 1 for rank in range(1, count + 1)]
    spread = 1 + sum(weights) // (1 << 30)
    return np.cumsum(np.array([max(1, weight // spread) for weight in weights]))


def ranked(rng, dims, number_of, slope):
    listing = cumulative_ranks(number_of, slope)
    ticket = jax.random.randint(jax.random.fold_in(rng, 1), dims, 0, int(listing[number_of - 1]))
    standing = jnp.searchsorted(jnp.asarray(listing, jnp.int32), ticket, side="right")
    return jax.random.permutation(jax.random.fold_in(rng, 2), number_of)[standing].astype(jnp.int32)


def bell_draw(rng, shape, scale, bound, shards=(), kind=jnp.bfloat16):
    values = jax.random.normal(rng, shape, jnp.float32) * scale
    if len(shards) > 0:
        values = shard_levels(rng, shape, shards, -0.22, 0.18) * values
    return jnp.clip(values, min=-bound, max=bound).astype(kind)


def setup_inputs(seed: int = 0) -> dict:
    arg_keys = jax.random.split(jax.random.key(seed), 6)
    return {
        "state": bell_draw(arg_keys[0], (4, NA, NT, CR), 1.0, 6.0, ((1, 2), (2, 16)), jnp.float32),
        "final_adjoint": bell_draw(arg_keys[1], (4, NA, NT, CR), 1.0, 6.0, ((1, 2), (2, 16)), jnp.float32),
        "resistance": jnp.clip(jnp.exp(jax.random.uniform(arg_keys[2], (PATCHES,), jnp.float32, math.log(0.2), math.log(2.0))), 0.2, 2.0),
        "wall_patch": set_ends(ranked(arg_keys[3], (NA, NT), PATCHES, 2), jax.random.fold_in(arg_keys[3], 3), 0, PATCHES - 1).astype(jnp.int32),
        "patch_slot_index": draw_patch_slot_index(jax.random.fold_in(arg_keys[5], 71), 0),
    }


mach_number = 0.5
time_step = 0.3


def axial_diff(field):
    padded = jnp.pad(field, ((0, 0), (1, 1), (0, 0), (0, 0)))
    return (padded[:, 2:] - padded[:, :-2]) * 0.5


def azim_diff(field):
    return (jnp.roll(field, -1, axis=2) - jnp.roll(field, 1, axis=2)) * 0.5


def radial_diff(field):
    padded = jnp.pad(field, ((0, 0), (0, 0), (0, 0), (1, 1)))
    return (padded[..., 2:] - padded[..., :-2]) * 0.5


def advance(field, liner_damping, orient):
    along = axial_diff(field)
    beside_all = azim_diff(field)
    radial = radial_diff(field)
    rate_press = orient * (-mach_number * along[0] - along[1] - beside_all[2] - radial[3]) - liner_damping * field[0]
    rate_axial = orient * (-mach_number * along[1] - along[0])
    rate_azim = orient * (-mach_number * along[2] - beside_all[0])
    rate_radial = orient * (-mach_number * along[3] - radial[0])
    rates = jnp.stack([rate_press, rate_axial, rate_azim, rate_radial], axis=0)
    return field + time_step * rates


def reference(state, final_adjoint, resistance, wall_patch, patch_slot_index):
    lined_wall_mask = (jnp.arange(CR) == CR - 1).astype(jnp.float32)
    liner_damping = resistance[wall_patch][:, :, None] * lined_wall_mask[None, None, :]
    field = state
    walls = []
    for step_index in range(ITERS):
        walls.append(field[0, :, :, CR - 1])
        field = advance(field, liner_damping, 1.0)
    adjoint = final_adjoint
    cell_grad = jnp.zeros((NA, NT), jnp.float32)
    for step_index in range(ITERS - 1, -1, -1):
        cell_grad = cell_grad - time_step * adjoint[0, :, :, CR - 1] * walls[step_index]
        adjoint = advance(adjoint, liner_damping, -1.0)
    partial_sums = jax.ops.segment_sum(cell_grad.reshape(-1), wall_patch.reshape(-1), PATCHES)
    patch_gradient = jnp.zeros((TOTAL_SLOT_COUNT,), jnp.float32).at[patch_slot_index].set(partial_sums)
    return adjoint, patch_gradient
```

```python
import jax
import jax.numpy as jnp
from jax import lax
from jax.sharding import PartitionSpec as P

ITERS = 4


mach_number = 0.5
time_step = 0.3


def halo(parts, axis, dim, width, closed):
    count = lax.axis_size(axis)
    ends = count if closed else count - 1
    heads = [lax.slice_in_dim(x, 0, width, axis=d) for x, d in zip(parts, dim)]
    tails = [lax.slice_in_dim(x, x.shape[d] - width, x.shape[d], axis=d) for x, d in zip(parts, dim)]
    from_lo = lax.ppermute(tails, axis, [(i, (i + 1) % count) for i in range(ends)])
    from_hi = lax.ppermute(heads, axis, [((i + 1) % count, i) for i in range(ends)])
    return [jnp.concatenate([lo, x, hi], axis=d) for lo, x, hi, d in zip(from_lo, parts, from_hi, dim)]


def radial_diff(component):
    zero_layer = jnp.zeros(component.shape[:-1] + (1,), component.dtype)
    upper = jnp.concatenate([component[..., 1:], zero_layer], axis=-1)
    lower = jnp.concatenate([zero_layer, component[..., :-1]], axis=-1)
    return (upper - lower) * 0.5


def advance(field, damping, row_mask, orient):
    centre = field[:, 1:-1, 1:-1]
    along = (field[:, 2:, 1:-1] - field[:, :-2, 1:-1]) * 0.5
    beside = (field[:, 1:-1, 2:] - field[:, 1:-1, :-2]) * 0.5
    radial_press = radial_diff(centre[0])
    radial_wall = radial_diff(centre[3])
    radial_count = field.shape[3]
    wall = (jnp.arange(radial_count) == radial_count - 1).astype(jnp.float32)
    liner = damping[1:-1, 1:-1, None] * wall[None, None, :]
    rate_press = (
        orient * (-mach_number * along[0] - along[1] - beside[2] - radial_wall)
        - liner * centre[0]
    )
    rate_axial = orient * (-mach_number * along[1] - along[0])
    rate_azim = orient * (-mach_number * along[2] - beside[0])
    rate_radial = orient * (-mach_number * along[3] - radial_press)
    rates = jnp.stack([rate_press, rate_axial, rate_azim, rate_radial], axis=0)
    keep = row_mask[1:-1, None, None]
    return (centre + time_step * rates) * keep[None]


def shards(state, final_adjoint, resistance, wall_patch, patch_slot_index):
    width = ITERS
    axial_local = state.shape[1]
    azim_local = state.shape[2]
    radial_count = state.shape[3]
    damping = resistance[wall_patch]
    state_p, adjoint_p, damping_p = halo(
        [state, final_adjoint, damping], "ax", [1, 1, 0], width, False
    )
    state_p, adjoint_p, damping_p = halo(
        [state_p, adjoint_p, damping_p], "az", [2, 2, 1], width, True
    )
    axial_total = axial_local * lax.axis_size("ax")
    first_row = lax.axis_index("ax") * axial_local - width
    rows = first_row + jnp.arange(axial_local + 2 * width)
    row_mask = ((rows >= 0) & (rows < axial_total)).astype(jnp.float32)

    def inner(x, margin):
        return x[..., margin : margin + axial_local, margin : margin + azim_local, :]

    walls = []
    field = state_p
    masks = row_mask
    damps = damping_p
    for step_index in range(ITERS):
        margin = width - step_index
        walls.append(inner(field[0], margin)[..., radial_count - 1])
        if step_index < ITERS - 1:
            field = advance(field, damps, masks, 1.0)
            masks = masks[1:-1]
            damps = damps[1:-1, 1:-1]
    adjoint = adjoint_p
    masks = row_mask
    damps = damping_p
    cell_grad = jnp.zeros((axial_local, azim_local), jnp.float32)
    for step_index in range(ITERS - 1, -1, -1):
        margin = width - (ITERS - 1 - step_index)
        cell_grad = cell_grad - time_step * inner(adjoint[0], margin)[..., radial_count - 1] * walls[step_index]
        adjoint = advance(adjoint, damps, masks, -1.0)
        masks = masks[1:-1]
        damps = damps[1:-1, 1:-1]
    slot_total = 2 * resistance.shape[0]
    cell_slot = patch_slot_index[wall_patch].reshape(-1)
    onehot = (cell_slot[:, None] == jnp.arange(slot_total, dtype=jnp.int32)[None, :]).astype(jnp.float32)
    slot_vector = jnp.dot(cell_grad.reshape(-1), onehot, precision=lax.Precision.HIGHEST)
    total = lax.psum(slot_vector, ("ax", "az"))
    owned = slot_total // lax.axis_size("az")
    patch_gradient = lax.dynamic_slice_in_dim(total, lax.axis_index("az") * owned, owned)
    return (adjoint, patch_gradient)


def solution(mesh):
    return jax.shard_map(
        shards,
        mesh=mesh,
        in_specs=(P(None, "ax", "az", None), P(None, "ax", "az", None), P(), P("ax", "az"), P()),
        out_specs=(P(None, "ax", "az", None), P("az")),
        check_vma=False,
    )
```

```python
import functools

import jax
import jax.numpy as jnp
from jax import lax
from jax.experimental import pallas as pl
from jax.experimental.pallas import tpu as pltpu
from jax.sharding import PartitionSpec as P

ITERS = 4


mach_number = 0.5
time_step = 0.3


def steps_kernel(
    axial_local, azim_local, radial_count, width, axial_total,
    axis_ref, state_ref, adjoint_ref, liner_ref, axial_lo_ref, axial_hi_ref, azim_ref,
    out_ref, grad_ref,
    field_a, field_b, adj_a, adj_b, liner_pad, walls,
):
    rows = axial_local + 2 * width
    cols = azim_local + 2 * width
    own = slice(width, width + axial_local)
    own_cols = slice(0, azim_local)

    for buf, lo in ((field_a, 0), (adj_a, 4)):
        buf[:, own, own_cols] = state_ref[...] if lo == 0 else adjoint_ref[...]
        buf[:, 0:width, own_cols] = axial_lo_ref[lo : lo + 4]
        buf[:, width + axial_local : rows, own_cols] = axial_hi_ref[lo : lo + 4]
        buf[:, :, azim_local:cols] = azim_ref[lo : lo + 4]
    liner_pad[own, own_cols] = liner_ref[...]
    liner_pad[0:width, own_cols] = axial_lo_ref[8]
    liner_pad[width + axial_local : rows, own_cols] = axial_hi_ref[8]
    liner_pad[:, azim_local:cols] = azim_ref[8]

    first_row = axis_ref[0] * axial_local - width
    lane = lax.broadcasted_iota(jnp.int32, (cols, radial_count), 1)
    not_last = lane != radial_count - 1
    not_first = lane != 0

    def radial_diff(x):
        upper = jnp.where(not_last, pltpu.roll(x, radial_count - 1, 1), 0.0)
        lower = jnp.where(not_first, pltpu.roll(x, 1, 1), 0.0)
        return (upper - lower) * 0.5

    def azim_diff(x):
        return (pltpu.roll(x, cols - 1, 0) - pltpu.roll(x, 1, 0)) * 0.5

    def advance(src, dst, step, orient):
        def body(r, carry):
            centre = src[:, r]
            along = (src[:, r + 1] - src[:, r - 1]) * 0.5
            press, axial, azim, radial = centre[0], centre[1], centre[2], centre[3]
            rate_press = (
                orient * (-mach_number * along[0] - along[1] - azim_diff(azim) - radial_diff(radial))
                - liner_pad[r] * press
            )
            rate_axial = orient * (-mach_number * along[1] - along[0])
            rate_azim = orient * (-mach_number * along[2] - azim_diff(press))
            rate_radial = orient * (-mach_number * along[3] - radial_diff(press))
            g = first_row + r
            keep = jnp.where((g >= 0) & (g < axial_total), 1.0, 0.0)
            dst[0, r] = (press + time_step * rate_press) * keep
            dst[1, r] = (axial + time_step * rate_axial) * keep
            dst[2, r] = (azim + time_step * rate_azim) * keep
            dst[3, r] = (radial + time_step * rate_radial) * keep
            return carry

        lax.fori_loop(step, rows - step, body, 0)

    walls[0] = state_ref[0]
    bufs = (field_a, field_b)
    for step in range(1, ITERS):
        advance(bufs[(step - 1) % 2], bufs[step % 2], step, 1.0)
        walls[step] = bufs[step % 2][0, own, own_cols]

    grad_ref[...] = jnp.zeros(grad_ref.shape, jnp.float32)
    bufs = (adj_a, adj_b)
    for step in range(1, ITERS + 1):
        grad_ref[...] = grad_ref[...] - time_step * bufs[(step - 1) % 2][0, own, own_cols] * walls[ITERS - step]
        advance(bufs[(step - 1) % 2], bufs[step % 2], step, -1.0)
    out_ref[...] = bufs[ITERS % 2][:, own, own_cols]


def shards(state, final_adjoint, resistance, wall_patch, patch_slot_index):
    width = ITERS
    axial_local = state.shape[1]
    azim_local = state.shape[2]
    radial_count = state.shape[3]
    wall = (jnp.arange(radial_count) == radial_count - 1).astype(jnp.float32)
    liner = resistance[wall_patch][:, :, None] * wall[None, None, :]

    def pack(sl_axis, start, stop):
        parts = [lax.slice_in_dim(x, start, stop, axis=sl_axis) for x in (state, final_adjoint)]
        parts.append(lax.slice_in_dim(liner, start, stop, axis=sl_axis - 1)[None])
        return jnp.concatenate(parts, axis=0)

    ax_count = lax.axis_size("ax")
    az_count = lax.axis_size("az")
    axial_lo, axial_hi = lax.ppermute(
        pack(1, axial_local - width, axial_local), "ax", [(i, i + 1) for i in range(ax_count - 1)]
    ), lax.ppermute(pack(1, 0, width), "ax", [(i + 1, i) for i in range(ax_count - 1)])

    def azim_pack(start, stop):
        return jnp.concatenate(
            [axial_lo[:, :, start:stop], pack(2, start, stop), axial_hi[:, :, start:stop]], axis=1
        )

    azim_prev = lax.ppermute(
        azim_pack(azim_local - width, azim_local), "az", [(i, (i + 1) % az_count) for i in range(az_count)]
    )
    azim_next = lax.ppermute(azim_pack(0, width), "az", [((i + 1) % az_count, i) for i in range(az_count)])
    azim_halo = jnp.concatenate([azim_next, azim_prev], axis=2)

    rows = axial_local + 2 * width
    cols = azim_local + 2 * width
    axis_index = jnp.reshape(lax.axis_index("ax"), (1,)).astype(jnp.int32)
    kernel = functools.partial(
        steps_kernel, axial_local, azim_local, radial_count, width, axial_local * ax_count
    )
    vmem = pl.BlockSpec(memory_space=pltpu.VMEM)
    adjoint, grad = pl.pallas_call(
        kernel,
        out_shape=(
            jax.ShapeDtypeStruct(state.shape, jnp.float32),
            jax.ShapeDtypeStruct((axial_local, azim_local, radial_count), jnp.float32),
        ),
        in_specs=[pl.BlockSpec(memory_space=pltpu.SMEM)] + [vmem] * 6,
        out_specs=(vmem, vmem),
        scratch_shapes=[pltpu.VMEM((4, rows, cols, radial_count), jnp.float32)] * 4
        + [
            pltpu.VMEM((rows, cols, radial_count), jnp.float32),
            pltpu.VMEM((ITERS, axial_local, azim_local, radial_count), jnp.float32),
        ],
    )(axis_index, state, final_adjoint, liner, axial_lo, axial_hi, azim_halo)
    cell_grad = grad[:, :, radial_count - 1]

    slot_total = 2 * resistance.shape[0]
    cell_slot = patch_slot_index[wall_patch].reshape(-1)
    onehot = (cell_slot[:, None] == jnp.arange(slot_total, dtype=jnp.int32)[None, :]).astype(jnp.float32)
    slot_vector = jnp.dot(cell_grad.reshape(-1), onehot, precision=lax.Precision.HIGHEST)
    total = lax.psum(slot_vector, ("ax", "az"))
    owned = slot_total // az_count
    patch_gradient = lax.dynamic_slice_in_dim(total, lax.axis_index("az") * owned, owned)
    return (adjoint, patch_gradient)


def solution(mesh):
    return jax.shard_map(
        shards,
        mesh=mesh,
        in_specs=(P(None, "ax", "az", None), P(None, "ax", "az", None), P(), P("ax", "az"), P()),
        out_specs=(P(None, "ax", "az", None), P("az")),
        check_vma=False,
    )
```

```python
import functools

import jax
import jax.numpy as jnp
from jax import lax
from jax.experimental import pallas as pl
from jax.experimental.pallas import tpu as pltpu
from jax.sharding import PartitionSpec as P

ITERS = 4


mach_number = 0.5
time_step = 0.3


def steps_kernel(
    axial_local, azim_local, radial_count, width, axial_total,
    axis_ref, state_ref, adjoint_ref, liner_ref, axial_lo_ref, axial_hi_ref, azim_ref,
    out_ref, grad_ref,
    field_a, field_b, adj_a, adj_b, liner_pad, walls,
):
    rows = axial_local + 2 * width
    cols = azim_local + 2 * width
    own = slice(width, width + axial_local)
    own_cols = slice(0, azim_local)

    for buf, lo in ((field_a, 0), (adj_a, 4)):
        buf[:, own, own_cols] = state_ref[...] if lo == 0 else adjoint_ref[...]
        buf[:, 0:width, own_cols] = axial_lo_ref[lo : lo + 4]
        buf[:, width + axial_local : rows, own_cols] = axial_hi_ref[lo : lo + 4]
        buf[:, :, azim_local:cols] = azim_ref[lo : lo + 4]
    liner_pad[own, own_cols] = liner_ref[...]
    liner_pad[0:width, own_cols] = axial_lo_ref[8]
    liner_pad[width + axial_local : rows, own_cols] = axial_hi_ref[8]
    liner_pad[:, azim_local:cols] = azim_ref[8]

    first_row = axis_ref[0] * axial_local - width
    lane = lax.broadcasted_iota(jnp.int32, (cols, radial_count), 1)
    not_last = lane != radial_count - 1
    not_first = lane != 0

    def radial_diff(x):
        upper = jnp.where(not_last, pltpu.roll(x, radial_count - 1, 1), 0.0)
        lower = jnp.where(not_first, pltpu.roll(x, 1, 1), 0.0)
        return (upper - lower) * 0.5

    def azim_diff(x):
        return (pltpu.roll(x, cols - 1, 0) - pltpu.roll(x, 1, 0)) * 0.5

    def advance(src, dst, step, orient):
        def body(r, carry):
            centre = src[:, r]
            along = (src[:, r + 1] - src[:, r - 1]) * 0.5
            press, axial, azim, radial = centre[0], centre[1], centre[2], centre[3]
            rate_press = (
                orient * (-mach_number * along[0] - along[1] - azim_diff(azim) - radial_diff(radial))
                - liner_pad[r] * press
            )
            rate_axial = orient * (-mach_number * along[1] - along[0])
            rate_azim = orient * (-mach_number * along[2] - azim_diff(press))
            rate_radial = orient * (-mach_number * along[3] - radial_diff(press))
            g = first_row + r
            keep = jnp.where((g >= 0) & (g < axial_total), 1.0, 0.0)
            dst[0, r] = (press + time_step * rate_press) * keep
            dst[1, r] = (axial + time_step * rate_axial) * keep
            dst[2, r] = (azim + time_step * rate_azim) * keep
            dst[3, r] = (radial + time_step * rate_radial) * keep
            return carry

        lax.fori_loop(step, rows - step, body, 0)

    walls[0] = state_ref[0]
    bufs = (field_a, field_b)
    for step in range(1, ITERS):
        advance(bufs[(step - 1) % 2], bufs[step % 2], step, 1.0)
        walls[step] = bufs[step % 2][0, own, own_cols]

    grad_ref[...] = jnp.zeros(grad_ref.shape, jnp.float32)
    bufs = (adj_a, adj_b)
    for step in range(1, ITERS + 1):
        grad_ref[...] = grad_ref[...] - time_step * bufs[(step - 1) % 2][0, own, own_cols] * walls[ITERS - step]
        advance(bufs[(step - 1) % 2], bufs[step % 2], step, -1.0)
    out_ref[...] = bufs[ITERS % 2][:, own, own_cols]


def shards(state, final_adjoint, resistance, wall_patch, patch_slot_index):
    width = ITERS
    axial_local = state.shape[1]
    azim_local = state.shape[2]
    radial_count = state.shape[3]
    wall = (jnp.arange(radial_count) == radial_count - 1).astype(jnp.float32)
    patch_count = resistance.shape[0]
    patch_onehot = (wall_patch[:, :, None] == jnp.arange(patch_count, dtype=jnp.int32)).astype(jnp.float32)
    damping = jnp.dot(patch_onehot, resistance, precision=lax.Precision.HIGHEST)
    liner = damping[:, :, None] * wall[None, None, :]

    def pack(sl_axis, start, stop):
        parts = [lax.slice_in_dim(x, start, stop, axis=sl_axis) for x in (state, final_adjoint)]
        parts.append(lax.slice_in_dim(liner, start, stop, axis=sl_axis - 1)[None])
        return jnp.concatenate(parts, axis=0)

    ax_count = lax.axis_size("ax")
    az_count = lax.axis_size("az")
    axial_lo, axial_hi = lax.ppermute(
        pack(1, axial_local - width, axial_local), "ax", [(i, i + 1) for i in range(ax_count - 1)]
    ), lax.ppermute(pack(1, 0, width), "ax", [(i + 1, i) for i in range(ax_count - 1)])

    def azim_pack(start, stop):
        return jnp.concatenate(
            [axial_lo[:, :, start:stop], pack(2, start, stop), axial_hi[:, :, start:stop]], axis=1
        )

    azim_prev = lax.ppermute(
        azim_pack(azim_local - width, azim_local), "az", [(i, (i + 1) % az_count) for i in range(az_count)]
    )
    azim_next = lax.ppermute(azim_pack(0, width), "az", [((i + 1) % az_count, i) for i in range(az_count)])
    azim_halo = jnp.concatenate([azim_next, azim_prev], axis=2)

    rows = axial_local + 2 * width
    cols = azim_local + 2 * width
    axis_index = jnp.reshape(lax.axis_index("ax"), (1,)).astype(jnp.int32)
    kernel = functools.partial(
        steps_kernel, axial_local, azim_local, radial_count, width, axial_local * ax_count
    )
    vmem = pl.BlockSpec(memory_space=pltpu.VMEM)
    adjoint, grad = pl.pallas_call(
        kernel,
        out_shape=(
            jax.ShapeDtypeStruct(state.shape, jnp.float32),
            jax.ShapeDtypeStruct((axial_local, azim_local, radial_count), jnp.float32),
        ),
        in_specs=[pl.BlockSpec(memory_space=pltpu.SMEM)] + [vmem] * 6,
        out_specs=(vmem, vmem),
        scratch_shapes=[pltpu.VMEM((4, rows, cols, radial_count), jnp.float32)] * 4
        + [
            pltpu.VMEM((rows, cols, radial_count), jnp.float32),
            pltpu.VMEM((ITERS, axial_local, azim_local, radial_count), jnp.float32),
        ],
    )(axis_index, state, final_adjoint, liner, axial_lo, axial_hi, azim_halo)
    cell_grad = grad[:, :, radial_count - 1]

    slot_total = 2 * resistance.shape[0]
    cell_slot = patch_slot_index[wall_patch].reshape(-1)
    onehot = (cell_slot[:, None] == jnp.arange(slot_total, dtype=jnp.int32)[None, :]).astype(jnp.float32)
    slot_vector = jnp.dot(cell_grad.reshape(-1), onehot, precision=lax.Precision.HIGHEST)
    owned = slot_total // az_count
    send = jnp.tile(slot_vector.reshape(az_count, owned), (ax_count, 1))
    patch_gradient = lax.all_to_all(send, ("ax", "az"), 0, 0, tiled=True).sum(0)
    return (adjoint, patch_gradient)


def solution(mesh):
    return jax.shard_map(
        shards,
        mesh=mesh,
        in_specs=(P(None, "ax", "az", None), P(None, "ax", "az", None), P(), P("ax", "az"), P()),
        out_specs=(P(None, "ax", "az", None), P("az")),
        check_vma=False,
    )
```

```python
import functools

import jax
import jax.numpy as jnp
from jax import lax
from jax.experimental import pallas as pl
from jax.experimental.pallas import tpu as pltpu
from jax.sharding import PartitionSpec as P

ITERS = 4
UNROLL = 4


mach_number = 0.5
time_step = 0.3


def steps_kernel(
    axial_local, azim_local, radial_count, width, axial_total,
    axis_ref, state_ref, adjoint_ref, liner_ref, axial_lo_ref, axial_hi_ref, azim_ref,
    out_ref, grad_ref,
    field_a, field_b, adj_a, adj_b, liner_pad, walls, adj_walls,
):
    rows = axial_local + 2 * width
    cols = azim_local + 2 * width
    own = slice(width, width + axial_local)
    own_cols = slice(0, azim_local)

    for buf, lo in ((field_a, 0), (adj_a, 4)):
        buf[:, own, own_cols] = state_ref[...] if lo == 0 else adjoint_ref[...]
        buf[:, 0:width, own_cols] = axial_lo_ref[lo : lo + 4]
        buf[:, width + axial_local : rows, own_cols] = axial_hi_ref[lo : lo + 4]
        buf[:, :, azim_local:cols] = azim_ref[lo : lo + 4]
    liner_pad[own, own_cols] = liner_ref[...]
    liner_pad[0:width, own_cols] = axial_lo_ref[8]
    liner_pad[width + axial_local : rows, own_cols] = axial_hi_ref[8]
    liner_pad[:, azim_local:cols] = azim_ref[8]

    first_row = axis_ref[0] * axial_local - width
    lane = lax.broadcasted_iota(jnp.int32, (cols, radial_count), 1)
    not_last = lane != radial_count - 1
    not_first = lane != 0

    def radial_diff(x):
        upper = jnp.where(not_last, pltpu.roll(x, radial_count - 1, 1), 0.0)
        lower = jnp.where(not_first, pltpu.roll(x, 1, 1), 0.0)
        return (upper - lower) * 0.5

    def azim_diff(x):
        return (pltpu.roll(x, cols - 1, 0) - pltpu.roll(x, 1, 0)) * 0.5

    def row(src, dst, r, orient, keep):
        centre = src[:, r]
        along = (src[:, r + 1] - src[:, r - 1]) * 0.5
        press, axial, azim, radial = centre[0], centre[1], centre[2], centre[3]
        rate_press = (
            orient * (-mach_number * along[0] - along[1] - azim_diff(azim) - radial_diff(radial))
            - liner_pad[r] * press
        )
        rate_axial = orient * (-mach_number * along[1] - along[0])
        rate_azim = orient * (-mach_number * along[2] - azim_diff(press))
        rate_radial = orient * (-mach_number * along[3] - radial_diff(press))
        dst[0, r] = (press + time_step * rate_press) * keep
        dst[1, r] = (axial + time_step * rate_axial) * keep
        dst[2, r] = (azim + time_step * rate_azim) * keep
        dst[3, r] = (radial + time_step * rate_radial) * keep

    def advance(chains, step):
        def body(r, carry):
            g = first_row + r
            keep = jnp.where((g >= 0) & (g < axial_total), 1.0, 0.0)
            for src, dst, orient in chains:
                row(src, dst, r, orient, keep)
            return carry

        lax.fori_loop(step, rows - step, body, 0, unroll=UNROLL)

    walls[0] = state_ref[0]
    adj_walls[0] = adjoint_ref[0]
    fwd = (field_a, field_b)
    adj = (adj_a, adj_b)
    for step in range(1, ITERS + 1):
        chains = [(adj[(step - 1) % 2], adj[step % 2], -1.0)]
        if step < ITERS:
            chains.append((fwd[(step - 1) % 2], fwd[step % 2], 1.0))
        advance(chains, step)
        if step < ITERS:
            walls[step] = fwd[step % 2][0, own, own_cols]
            adj_walls[step] = adj[step % 2][0, own, own_cols]

    grad = jnp.zeros(grad_ref.shape, jnp.float32)
    for step in range(1, ITERS + 1):
        grad = grad - time_step * adj_walls[step - 1] * walls[ITERS - step]
    grad_ref[...] = grad
    out_ref[...] = adj[ITERS % 2][:, own, own_cols]


def shards(state, final_adjoint, resistance, wall_patch, patch_slot_index):
    width = ITERS
    axial_local = state.shape[1]
    azim_local = state.shape[2]
    radial_count = state.shape[3]
    wall = (jnp.arange(radial_count) == radial_count - 1).astype(jnp.float32)
    patch_count = resistance.shape[0]
    patch_onehot = (wall_patch[:, :, None] == jnp.arange(patch_count, dtype=jnp.int32)).astype(jnp.float32)
    damping = jnp.dot(patch_onehot, resistance, precision=lax.Precision.HIGHEST)
    liner = damping[:, :, None] * wall[None, None, :]

    def pack(sl_axis, start, stop):
        parts = [lax.slice_in_dim(x, start, stop, axis=sl_axis) for x in (state, final_adjoint)]
        parts.append(lax.slice_in_dim(liner, start, stop, axis=sl_axis - 1)[None])
        return jnp.concatenate(parts, axis=0)

    ax_count = lax.axis_size("ax")
    az_count = lax.axis_size("az")
    axial_lo, axial_hi = lax.ppermute(
        pack(1, axial_local - width, axial_local), "ax", [(i, i + 1) for i in range(ax_count - 1)]
    ), lax.ppermute(pack(1, 0, width), "ax", [(i + 1, i) for i in range(ax_count - 1)])

    def azim_pack(start, stop):
        return jnp.concatenate(
            [axial_lo[:, :, start:stop], pack(2, start, stop), axial_hi[:, :, start:stop]], axis=1
        )

    azim_prev = lax.ppermute(
        azim_pack(azim_local - width, azim_local), "az", [(i, (i + 1) % az_count) for i in range(az_count)]
    )
    azim_next = lax.ppermute(azim_pack(0, width), "az", [((i + 1) % az_count, i) for i in range(az_count)])
    azim_halo = jnp.concatenate([azim_next, azim_prev], axis=2)

    rows = axial_local + 2 * width
    cols = azim_local + 2 * width
    axis_index = jnp.reshape(lax.axis_index("ax"), (1,)).astype(jnp.int32)
    kernel = functools.partial(
        steps_kernel, axial_local, azim_local, radial_count, width, axial_local * ax_count
    )
    vmem = pl.BlockSpec(memory_space=pltpu.VMEM)
    adjoint, grad = pl.pallas_call(
        kernel,
        out_shape=(
            jax.ShapeDtypeStruct(state.shape, jnp.float32),
            jax.ShapeDtypeStruct((axial_local, azim_local, radial_count), jnp.float32),
        ),
        in_specs=[pl.BlockSpec(memory_space=pltpu.SMEM)] + [vmem] * 6,
        out_specs=(vmem, vmem),
        scratch_shapes=[pltpu.VMEM((4, rows, cols, radial_count), jnp.float32)] * 4
        + [
            pltpu.VMEM((rows, cols, radial_count), jnp.float32),
            pltpu.VMEM((ITERS, axial_local, azim_local, radial_count), jnp.float32),
            pltpu.VMEM((ITERS, axial_local, azim_local, radial_count), jnp.float32),
        ],
    )(axis_index, state, final_adjoint, liner, axial_lo, axial_hi, azim_halo)
    cell_grad = grad[:, :, radial_count - 1]

    slot_total = 2 * resistance.shape[0]
    cell_slot = patch_slot_index[wall_patch].reshape(-1)
    onehot = (cell_slot[:, None] == jnp.arange(slot_total, dtype=jnp.int32)[None, :]).astype(jnp.float32)
    slot_vector = jnp.dot(cell_grad.reshape(-1), onehot, precision=lax.Precision.HIGHEST)
    owned = slot_total // az_count
    send = jnp.tile(slot_vector.reshape(az_count, owned), (ax_count, 1))
    patch_gradient = lax.all_to_all(send, ("ax", "az"), 0, 0, tiled=True).sum(0)
    return (adjoint, patch_gradient)


def solution(mesh):
    return jax.shard_map(
        shards,
        mesh=mesh,
        in_specs=(P(None, "ax", "az", None), P(None, "ax", "az", None), P(), P("ax", "az"), P()),
        out_specs=(P(None, "ax", "az", None), P("az")),
        check_vma=False,
    )
```

```python
import functools

import jax
import jax.numpy as jnp
from jax import lax
from jax.experimental import pallas as pl
from jax.experimental.pallas import tpu as pltpu
from jax.sharding import PartitionSpec as P

ITERS = 4
UNROLL = 4


mach_number = 0.5
time_step = 0.3


def steps_kernel(
    axial_local, azim_local, radial_count, width, axial_total,
    axis_ref, state_ref, adjoint_ref, liner_ref,
    state_lo_ref, state_hi_ref, adj_lo_ref, adj_hi_ref,
    state_next_ref, state_prev_ref, adj_next_ref, adj_prev_ref,
    out_ref, grad_ref,
    field_a, field_b, adj_a, adj_b, walls, adj_walls,
):
    rows = axial_local + 2 * width
    cols = azim_local + 2 * width
    own = slice(width, width + axial_local)
    own_cols = slice(0, azim_local)
    liner_pad = liner_ref
    narrow = width - 1

    field_a[...] = jnp.zeros(field_a.shape, jnp.float32)
    field_a[:, own, own_cols] = state_ref[...]
    field_a[:, 1:width, own_cols] = state_lo_ref[...]
    field_a[:, width + axial_local : rows - 1, own_cols] = state_hi_ref[...]
    field_a[:, 1 : rows - 1, azim_local : azim_local + narrow] = state_next_ref[...]
    field_a[:, 1 : rows - 1, cols - narrow : cols] = state_prev_ref[...]
    adj_a[:, own, own_cols] = adjoint_ref[...]
    adj_a[:, 0:width, own_cols] = adj_lo_ref[...]
    adj_a[:, width + axial_local : rows, own_cols] = adj_hi_ref[...]
    adj_a[:, :, azim_local : azim_local + width] = adj_next_ref[...]
    adj_a[:, :, azim_local + width : cols] = adj_prev_ref[...]

    first_row = axis_ref[0] * axial_local - width
    lane = lax.broadcasted_iota(jnp.int32, (cols, radial_count), 1)
    not_last = lane != radial_count - 1
    not_first = lane != 0

    def radial_diff(x):
        upper = jnp.where(not_last, pltpu.roll(x, radial_count - 1, 1), 0.0)
        lower = jnp.where(not_first, pltpu.roll(x, 1, 1), 0.0)
        return (upper - lower) * 0.5

    def azim_diff(x):
        return (pltpu.roll(x, cols - 1, 0) - pltpu.roll(x, 1, 0)) * 0.5

    def row(src, dst, r, orient, keep):
        centre = src[:, r]
        along = (src[:, r + 1] - src[:, r - 1]) * 0.5
        press, axial, azim, radial = centre[0], centre[1], centre[2], centre[3]
        rate_press = (
            orient * (-mach_number * along[0] - along[1] - azim_diff(azim) - radial_diff(radial))
            - liner_pad[r] * press
        )
        rate_axial = orient * (-mach_number * along[1] - along[0])
        rate_azim = orient * (-mach_number * along[2] - azim_diff(press))
        rate_radial = orient * (-mach_number * along[3] - radial_diff(press))
        dst[0, r] = (press + time_step * rate_press) * keep
        dst[1, r] = (axial + time_step * rate_axial) * keep
        dst[2, r] = (azim + time_step * rate_azim) * keep
        dst[3, r] = (radial + time_step * rate_radial) * keep

    def advance(chains, step):
        def body(r, carry):
            g = first_row + r
            keep = jnp.where((g >= 0) & (g < axial_total), 1.0, 0.0)
            for src, dst, orient in chains:
                row(src, dst, r, orient, keep)
            return carry

        lax.fori_loop(step, rows - step, body, 0, unroll=UNROLL)

    walls[0] = state_ref[0]
    adj_walls[0] = adjoint_ref[0]
    fwd = (field_a, field_b)
    adj = (adj_a, adj_b)
    for step in range(1, ITERS + 1):
        chains = [(adj[(step - 1) % 2], adj[step % 2], -1.0)]
        if step < ITERS:
            chains.append((fwd[(step - 1) % 2], fwd[step % 2], 1.0))
        advance(chains, step)
        if step < ITERS:
            walls[step] = fwd[step % 2][0, own, own_cols]
            adj_walls[step] = adj[step % 2][0, own, own_cols]

    grad = jnp.zeros(grad_ref.shape, jnp.float32)
    for step in range(1, ITERS + 1):
        grad = grad - time_step * adj_walls[step - 1] * walls[ITERS - step]
    grad_ref[...] = grad
    out_ref[...] = adj[ITERS % 2][:, own, own_cols]


def shards(state, final_adjoint, resistance, wall_patch, patch_slot_index):
    width = ITERS
    axial_local = state.shape[1]
    azim_local = state.shape[2]
    radial_count = state.shape[3]
    narrow = width - 1
    ax_count = lax.axis_size("ax")
    az_count = lax.axis_size("az")
    up_ax = [(i, i + 1) for i in range(ax_count - 1)]
    down_ax = [(i + 1, i) for i in range(ax_count - 1)]
    up_az = [(i, (i + 1) % az_count) for i in range(az_count)]
    down_az = [((i + 1) % az_count, i) for i in range(az_count)]

    def tail(x, dim, n):
        return lax.slice_in_dim(x, x.shape[dim] - n, x.shape[dim], axis=dim)

    def head(x, dim, n):
        return lax.slice_in_dim(x, 0, n, axis=dim)

    state_lo = lax.ppermute(tail(state, 1, narrow), "ax", up_ax)
    adj_lo = lax.ppermute(tail(final_adjoint, 1, width), "ax", up_ax)
    state_hi = lax.ppermute(head(state, 1, narrow), "ax", down_ax)
    adj_hi = lax.ppermute(head(final_adjoint, 1, width), "ax", down_ax)

    patch_count = resistance.shape[0]
    patch_onehot = (wall_patch[:, :, None] == jnp.arange(patch_count, dtype=jnp.int32)).astype(jnp.float32)
    damping = jnp.dot(patch_onehot, resistance, precision=lax.Precision.HIGHEST)
    damp_lo = lax.ppermute(tail(damping, 0, width), "ax", up_ax)
    damp_hi = lax.ppermute(head(damping, 0, width), "ax", down_ax)

    state_rows = jnp.concatenate([state_lo, state, state_hi], axis=1)
    adj_rows = jnp.concatenate([adj_lo, final_adjoint, adj_hi], axis=1)
    damp_rows = jnp.concatenate([damp_lo, damping, damp_hi], axis=0)
    state_prev = lax.ppermute(tail(state_rows, 2, narrow), "az", up_az)
    adj_prev = lax.ppermute(tail(adj_rows, 2, width), "az", up_az)
    state_next = lax.ppermute(head(state_rows, 2, narrow), "az", down_az)
    adj_next = lax.ppermute(head(adj_rows, 2, width), "az", down_az)
    damp_prev = lax.ppermute(tail(damp_rows, 1, width), "az", up_az)
    damp_next = lax.ppermute(head(damp_rows, 1, width), "az", down_az)
    damp_pad = jnp.concatenate([damp_rows, damp_next, damp_prev], axis=1)
    wall = (jnp.arange(radial_count) == radial_count - 1).astype(jnp.float32)
    liner_pad = damp_pad[:, :, None] * wall[None, None, :]

    rows = axial_local + 2 * width
    cols = azim_local + 2 * width
    axis_index = jnp.reshape(lax.axis_index("ax"), (1,)).astype(jnp.int32)
    kernel = functools.partial(
        steps_kernel, axial_local, azim_local, radial_count, width, axial_local * ax_count
    )
    vmem = pl.BlockSpec(memory_space=pltpu.VMEM)
    adjoint, grad = pl.pallas_call(
        kernel,
        out_shape=(
            jax.ShapeDtypeStruct(state.shape, jnp.float32),
            jax.ShapeDtypeStruct((axial_local, azim_local, radial_count), jnp.float32),
        ),
        in_specs=[pl.BlockSpec(memory_space=pltpu.SMEM)] + [vmem] * 11,
        out_specs=(vmem, vmem),
        scratch_shapes=[pltpu.VMEM((4, rows, cols, radial_count), jnp.float32)] * 4
        + [
            pltpu.VMEM((ITERS, axial_local, azim_local, radial_count), jnp.float32),
            pltpu.VMEM((ITERS, axial_local, azim_local, radial_count), jnp.float32),
        ],
    )(
        axis_index, state, final_adjoint, liner_pad,
        state_lo, state_hi, adj_lo, adj_hi,
        state_next, state_prev, adj_next, adj_prev,
    )
    cell_grad = grad[:, :, radial_count - 1]

    slot_total = 2 * resistance.shape[0]
    cell_slot = patch_slot_index[wall_patch].reshape(-1)
    onehot = (cell_slot[:, None] == jnp.arange(slot_total, dtype=jnp.int32)[None, :]).astype(jnp.float32)
    slot_vector = jnp.dot(cell_grad.reshape(-1), onehot, precision=lax.Precision.HIGHEST)
    owned = slot_total // az_count
    send = jnp.tile(slot_vector.reshape(az_count, owned), (ax_count, 1))
    patch_gradient = lax.all_to_all(send, ("ax", "az"), 0, 0, tiled=True).sum(0)
    return (adjoint, patch_gradient)


def solution(mesh):
    return jax.shard_map(
        shards,
        mesh=mesh,
        in_specs=(P(None, "ax", "az", None), P(None, "ax", "az", None), P(), P("ax", "az"), P()),
        out_specs=(P(None, "ax", "az", None), P("az")),
        check_vma=False,
    )
```

```python
import functools

import jax
import jax.numpy as jnp
from jax import lax
from jax.experimental import pallas as pl
from jax.experimental.pallas import tpu as pltpu
from jax.sharding import PartitionSpec as P

ITERS = 4
UNROLL = 4


mach_number = 0.5
time_step = 0.3


def steps_kernel(
    axial_local, azim_local, radial_count, width, axial_total,
    axis_ref, state_ref, adjoint_ref, liner_ref, axial_lo_ref, axial_hi_ref, azim_next_ref, azim_prev_ref,
    out_ref, grad_ref,
    field_a, field_b, adj_a, adj_b, liner_pad, walls, adj_walls,
):
    rows = axial_local + 2 * width
    cols = azim_local + 2 * width
    own = slice(width, width + axial_local)
    own_cols = slice(0, azim_local)

    far = width - 1
    halo_cols = slice(azim_local, cols)
    for buf in (field_a, adj_a):
        buf[:, 0, halo_cols] = jnp.zeros((4, 2 * width, radial_count), jnp.float32)
        buf[:, rows - 1, halo_cols] = jnp.zeros((4, 2 * width, radial_count), jnp.float32)
    field_a[:, :, azim_local + far : azim_local + width + 1] = jnp.zeros((4, rows, 2, radial_count), jnp.float32)
    liner_pad[...] = jnp.zeros(liner_pad.shape, jnp.float32)
    for buf, lo in ((field_a, 0), (adj_a, 4)):
        buf[:, own, own_cols] = state_ref[...] if lo == 0 else adjoint_ref[...]
        buf[:, 0:width, own_cols] = axial_lo_ref[lo : lo + 4]
        buf[:, width + axial_local : rows, own_cols] = axial_hi_ref[lo : lo + 4]
    inner = slice(1, rows - 1)
    adj_a[:, inner, azim_local : azim_local + width] = azim_next_ref[:, :, 0:width]
    adj_a[:, inner, azim_local + width : cols] = azim_prev_ref[:, :, 0:width]
    field_a[:, inner, azim_local : azim_local + far] = azim_next_ref[:, :, width : width + far]
    field_a[:, inner, cols - far : cols] = azim_prev_ref[:, :, width : width + far]
    liner_pad[own, own_cols] = liner_ref[...]
    liner_pad[0:width, own_cols] = axial_lo_ref[8]
    liner_pad[width + axial_local : rows, own_cols] = axial_hi_ref[8]
    strip_lane = lax.broadcasted_iota(jnp.int32, (rows - 2, 1, radial_count), 2)
    next_damp = azim_next_ref[1, :, far : far + 1, :]
    prev_damp = azim_prev_ref[1, :, 0:1, :]
    for m in range(far):
        col = azim_local + m
        liner_pad[inner, col : col + 1] = jnp.where(
            strip_lane == radial_count - 1, pltpu.roll(next_damp, radial_count - 1 - m, 2), 0.0
        )
        col = cols - far + m
        liner_pad[inner, col : col + 1] = jnp.where(
            strip_lane == radial_count - 1, pltpu.roll(prev_damp, radial_count - 1 - m, 2), 0.0
        )

    first_row = axis_ref[0] * axial_local - width
    lane = lax.broadcasted_iota(jnp.int32, (cols, radial_count), 1)
    not_last = lane != radial_count - 1
    not_first = lane != 0

    def radial_diff(x):
        upper = jnp.where(not_last, pltpu.roll(x, radial_count - 1, 1), 0.0)
        lower = jnp.where(not_first, pltpu.roll(x, 1, 1), 0.0)
        return (upper - lower) * 0.5

    def azim_diff(x):
        return (pltpu.roll(x, cols - 1, 0) - pltpu.roll(x, 1, 0)) * 0.5

    def row(src, dst, r, orient, keep):
        centre = src[:, r]
        along = (src[:, r + 1] - src[:, r - 1]) * 0.5
        press, axial, azim, radial = centre[0], centre[1], centre[2], centre[3]
        rate_press = (
            orient * (-mach_number * along[0] - along[1] - azim_diff(azim) - radial_diff(radial))
            - liner_pad[r] * press
        )
        rate_axial = orient * (-mach_number * along[1] - along[0])
        rate_azim = orient * (-mach_number * along[2] - azim_diff(press))
        rate_radial = orient * (-mach_number * along[3] - radial_diff(press))
        dst[0, r] = (press + time_step * rate_press) * keep
        dst[1, r] = (axial + time_step * rate_axial) * keep
        dst[2, r] = (azim + time_step * rate_azim) * keep
        dst[3, r] = (radial + time_step * rate_radial) * keep

    def advance(chains, step):
        def body(r, carry):
            g = first_row + r
            keep = jnp.where((g >= 0) & (g < axial_total), 1.0, 0.0)
            for src, dst, orient in chains:
                row(src, dst, r, orient, keep)
            return carry

        lax.fori_loop(step, rows - step, body, 0, unroll=UNROLL)

    walls[0] = state_ref[0]
    adj_walls[0] = adjoint_ref[0]
    fwd = (field_a, field_b)
    adj = (adj_a, adj_b)
    for step in range(1, ITERS + 1):
        chains = [(adj[(step - 1) % 2], adj[step % 2], -1.0)]
        if step < ITERS:
            chains.append((fwd[(step - 1) % 2], fwd[step % 2], 1.0))
        advance(chains, step)
        if step < ITERS:
            walls[step] = fwd[step % 2][0, own, own_cols]
            adj_walls[step] = adj[step % 2][0, own, own_cols]

    grad = jnp.zeros(grad_ref.shape, jnp.float32)
    for step in range(1, ITERS + 1):
        grad = grad - time_step * adj_walls[step - 1] * walls[ITERS - step]
    grad_ref[...] = grad
    out_ref[...] = adj[ITERS % 2][:, own, own_cols]


def shards(state, final_adjoint, resistance, wall_patch, patch_slot_index):
    width = ITERS
    axial_local = state.shape[1]
    azim_local = state.shape[2]
    radial_count = state.shape[3]
    wall = (jnp.arange(radial_count) == radial_count - 1).astype(jnp.float32)
    patch_count = resistance.shape[0]
    patch_onehot = (wall_patch[:, :, None] == jnp.arange(patch_count, dtype=jnp.int32)).astype(jnp.float32)
    damping = jnp.dot(patch_onehot, resistance, precision=lax.Precision.HIGHEST)
    liner = damping[:, :, None] * wall[None, None, :]

    def pack(sl_axis, start, stop):
        parts = [lax.slice_in_dim(x, start, stop, axis=sl_axis) for x in (state, final_adjoint)]
        parts.append(lax.slice_in_dim(liner, start, stop, axis=sl_axis - 1)[None])
        return jnp.concatenate(parts, axis=0)

    ax_count = lax.axis_size("ax")
    az_count = lax.axis_size("az")
    axial_lo, axial_hi = lax.ppermute(
        pack(1, axial_local - width, axial_local), "ax", [(i, i + 1) for i in range(ax_count - 1)]
    ), lax.ppermute(pack(1, 0, width), "ax", [(i + 1, i) for i in range(ax_count - 1)])

    far = width - 1

    def padded_rows(lo, own_block, hi):
        return jnp.concatenate([lo[:, 1:], own_block, hi[:, :-1]], axis=1)

    state_rows = padded_rows(axial_lo[0:4], state, axial_hi[0:4])
    adj_rows = padded_rows(axial_lo[4:8], final_adjoint, axial_hi[4:8])
    damp_rows = jnp.concatenate(
        [axial_lo[8, 1:, :, radial_count - 1], damping, axial_hi[8, :-1, :, radial_count - 1]], axis=0
    )

    def lanes(x):
        return jnp.pad(x, ((0, 0), (0, radial_count - x.shape[1])))

    next_pack = jnp.concatenate([adj_rows[:, :, 0:width], state_rows[:, :, 0:far]], axis=2)
    next_pack = next_pack.at[1, :, far].set(lanes(damp_rows[:, 0:far]))
    prev_pack = jnp.concatenate(
        [adj_rows[:, :, azim_local - width :], state_rows[:, :, azim_local - far :]], axis=2
    )
    prev_pack = prev_pack.at[1, :, 0].set(lanes(damp_rows[:, azim_local - far :]))
    azim_prev = lax.ppermute(prev_pack, "az", [(i, (i + 1) % az_count) for i in range(az_count)])
    azim_next = lax.ppermute(next_pack, "az", [((i + 1) % az_count, i) for i in range(az_count)])

    rows = axial_local + 2 * width
    cols = azim_local + 2 * width
    axis_index = jnp.reshape(lax.axis_index("ax"), (1,)).astype(jnp.int32)
    kernel = functools.partial(
        steps_kernel, axial_local, azim_local, radial_count, width, axial_local * ax_count
    )
    vmem = pl.BlockSpec(memory_space=pltpu.VMEM)
    adjoint, grad = pl.pallas_call(
        kernel,
        out_shape=(
            jax.ShapeDtypeStruct(state.shape, jnp.float32),
            jax.ShapeDtypeStruct((axial_local, azim_local, radial_count), jnp.float32),
        ),
        in_specs=[pl.BlockSpec(memory_space=pltpu.SMEM)] + [vmem] * 7,
        out_specs=(vmem, vmem),
        scratch_shapes=[pltpu.VMEM((4, rows, cols, radial_count), jnp.float32)] * 4
        + [
            pltpu.VMEM((rows, cols, radial_count), jnp.float32),
            pltpu.VMEM((ITERS, axial_local, azim_local, radial_count), jnp.float32),
            pltpu.VMEM((ITERS, axial_local, azim_local, radial_count), jnp.float32),
        ],
    )(axis_index, state, final_adjoint, liner, axial_lo, axial_hi, azim_next, azim_prev)
    cell_grad = grad[:, :, radial_count - 1]

    slot_total = 2 * resistance.shape[0]
    cell_slot = patch_slot_index[wall_patch].reshape(-1)
    onehot = (cell_slot[:, None] == jnp.arange(slot_total, dtype=jnp.int32)[None, :]).astype(jnp.float32)
    slot_vector = jnp.dot(cell_grad.reshape(-1), onehot, precision=lax.Precision.HIGHEST)
    owned = slot_total // az_count
    send = jnp.tile(slot_vector.reshape(az_count, owned), (ax_count, 1))
    patch_gradient = lax.all_to_all(send, ("ax", "az"), 0, 0, tiled=True).sum(0)
    return (adjoint, patch_gradient)


def solution(mesh):
    return jax.shard_map(
        shards,
        mesh=mesh,
        in_specs=(P(None, "ax", "az", None), P(None, "ax", "az", None), P(), P("ax", "az"), P()),
        out_specs=(P(None, "ax", "az", None), P("az")),
        check_vma=False,
    )
```

```python
import functools

import jax
import jax.numpy as jnp
from jax import lax
from jax.experimental import pallas as pl
from jax.experimental.pallas import tpu as pltpu
from jax.sharding import PartitionSpec as P

ITERS = 4
UNROLL = 4


mach_number = 0.5
time_step = 0.3


def steps_kernel(
    axial_local, azim_local, radial_count, width, axial_total,
    axis_ref, state_ref, adjoint_ref, liner_ref, axial_lo_ref, axial_hi_ref, azim_next_ref, azim_prev_ref,
    owner_ref, place_ref,
    out_ref, send_ref,
    field_a, field_b, adj_a, adj_b, liner_pad, walls, adj_walls,
):
    rows = axial_local + 2 * width
    cols = azim_local + 2 * width
    own = slice(width, width + axial_local)
    own_cols = slice(0, azim_local)

    far = width - 1
    halo_cols = slice(azim_local, cols)
    for buf in (field_a, adj_a):
        buf[:, 0, halo_cols] = jnp.zeros((4, 2 * width, radial_count), jnp.float32)
        buf[:, rows - 1, halo_cols] = jnp.zeros((4, 2 * width, radial_count), jnp.float32)
    field_a[:, :, azim_local + far : azim_local + width + 1] = jnp.zeros((4, rows, 2, radial_count), jnp.float32)
    liner_pad[...] = jnp.zeros(liner_pad.shape, jnp.float32)
    for buf, lo in ((field_a, 0), (adj_a, 4)):
        buf[:, own, own_cols] = state_ref[...] if lo == 0 else adjoint_ref[...]
        buf[:, 0:width, own_cols] = axial_lo_ref[lo : lo + 4]
        buf[:, width + axial_local : rows, own_cols] = axial_hi_ref[lo : lo + 4]
    inner = slice(1, rows - 1)
    adj_a[:, inner, azim_local : azim_local + width] = azim_next_ref[:, :, 0:width]
    adj_a[:, inner, azim_local + width : cols] = azim_prev_ref[:, :, 0:width]
    field_a[:, inner, azim_local : azim_local + far] = azim_next_ref[:, :, width : width + far]
    field_a[:, inner, cols - far : cols] = azim_prev_ref[:, :, width : width + far]
    liner_pad[own, own_cols] = liner_ref[...]
    liner_pad[0:width, own_cols] = axial_lo_ref[8]
    liner_pad[width + axial_local : rows, own_cols] = axial_hi_ref[8]
    strip_lane = lax.broadcasted_iota(jnp.int32, (rows - 2, 1, radial_count), 2)
    next_damp = azim_next_ref[1, :, far : far + 1, :]
    prev_damp = azim_prev_ref[1, :, 0:1, :]
    for m in range(far):
        col = azim_local + m
        liner_pad[inner, col : col + 1] = jnp.where(
            strip_lane == radial_count - 1, pltpu.roll(next_damp, radial_count - 1 - m, 2), 0.0
        )
        col = cols - far + m
        liner_pad[inner, col : col + 1] = jnp.where(
            strip_lane == radial_count - 1, pltpu.roll(prev_damp, radial_count - 1 - m, 2), 0.0
        )

    first_row = axis_ref[0] * axial_local - width
    lane = lax.broadcasted_iota(jnp.int32, (cols, radial_count), 1)
    not_last = lane != radial_count - 1
    not_first = lane != 0

    def radial_diff(x):
        upper = jnp.where(not_last, pltpu.roll(x, radial_count - 1, 1), 0.0)
        lower = jnp.where(not_first, pltpu.roll(x, 1, 1), 0.0)
        return (upper - lower) * 0.5

    def azim_diff(x):
        return (pltpu.roll(x, cols - 1, 0) - pltpu.roll(x, 1, 0)) * 0.5

    def row(src, dst, r, orient, keep):
        centre = src[:, r]
        along = (src[:, r + 1] - src[:, r - 1]) * 0.5
        press, axial, azim, radial = centre[0], centre[1], centre[2], centre[3]
        rate_press = (
            orient * (-mach_number * along[0] - along[1] - azim_diff(azim) - radial_diff(radial))
            - liner_pad[r] * press
        )
        rate_axial = orient * (-mach_number * along[1] - along[0])
        rate_azim = orient * (-mach_number * along[2] - azim_diff(press))
        rate_radial = orient * (-mach_number * along[3] - radial_diff(press))
        dst[0, r] = (press + time_step * rate_press) * keep
        dst[1, r] = (axial + time_step * rate_axial) * keep
        dst[2, r] = (azim + time_step * rate_azim) * keep
        dst[3, r] = (radial + time_step * rate_radial) * keep

    def advance(chains, step):
        def body(r, carry):
            g = first_row + r
            keep = jnp.where((g >= 0) & (g < axial_total), 1.0, 0.0)
            for src, dst, orient in chains:
                row(src, dst, r, orient, keep)
            return carry

        lax.fori_loop(step, rows - step, body, 0, unroll=UNROLL)

    walls[0] = state_ref[0]
    adj_walls[0] = adjoint_ref[0]
    fwd = (field_a, field_b)
    adj = (adj_a, adj_b)
    for step in range(1, ITERS + 1):
        chains = [(adj[(step - 1) % 2], adj[step % 2], -1.0)]
        if step < ITERS:
            chains.append((fwd[(step - 1) % 2], fwd[step % 2], 1.0))
        advance(chains, step)
        if step < ITERS:
            walls[step] = fwd[step % 2][0, own, own_cols]
            adj_walls[step] = adj[step % 2][0, own, own_cols]

    grad = jnp.zeros(walls.shape[1:], jnp.float32)
    for step in range(1, ITERS + 1):
        grad = grad - time_step * adj_walls[step - 1] * walls[ITERS - step]
    by_cell = grad.reshape(axial_local * azim_local, radial_count)
    wall_lane = (lax.broadcasted_iota(jnp.int32, (8, radial_count), 1) == radial_count - 1).astype(jnp.float32)
    cell_row = lax.dot_general(
        wall_lane, by_cell, (((1,), (1,)), ((), ())),
        precision=lax.Precision.HIGHEST, preferred_element_type=jnp.float32,
    )[0:1]
    send_ref[...] = jnp.dot(
        owner_ref[...] * cell_row, place_ref[...],
        precision=lax.Precision.HIGHEST, preferred_element_type=jnp.float32,
    )
    out_ref[...] = adj[ITERS % 2][:, own, own_cols]


def shards(state, final_adjoint, resistance, wall_patch, patch_slot_index):
    width = ITERS
    axial_local = state.shape[1]
    azim_local = state.shape[2]
    radial_count = state.shape[3]
    wall = (jnp.arange(radial_count) == radial_count - 1).astype(jnp.float32)
    patch_count = resistance.shape[0]
    patch_onehot = (wall_patch[:, :, None] == jnp.arange(patch_count, dtype=jnp.int32)).astype(jnp.float32)
    damping = jnp.dot(patch_onehot, resistance, precision=lax.Precision.HIGHEST)
    liner = damping[:, :, None] * wall[None, None, :]

    def pack(sl_axis, start, stop):
        parts = [lax.slice_in_dim(x, start, stop, axis=sl_axis) for x in (state, final_adjoint)]
        parts.append(lax.slice_in_dim(liner, start, stop, axis=sl_axis - 1)[None])
        return jnp.concatenate(parts, axis=0)

    ax_count = lax.axis_size("ax")
    az_count = lax.axis_size("az")
    axial_lo, axial_hi = lax.ppermute(
        pack(1, axial_local - width, axial_local), "ax", [(i, i + 1) for i in range(ax_count - 1)]
    ), lax.ppermute(pack(1, 0, width), "ax", [(i + 1, i) for i in range(ax_count - 1)])

    far = width - 1

    def padded_rows(lo, own_block, hi):
        return jnp.concatenate([lo[:, 1:], own_block, hi[:, :-1]], axis=1)

    state_rows = padded_rows(axial_lo[0:4], state, axial_hi[0:4])
    adj_rows = padded_rows(axial_lo[4:8], final_adjoint, axial_hi[4:8])
    damp_rows = jnp.concatenate(
        [axial_lo[8, 1:, :, radial_count - 1], damping, axial_hi[8, :-1, :, radial_count - 1]], axis=0
    )

    def lanes(x):
        return jnp.pad(x, ((0, 0), (0, radial_count - x.shape[1])))

    next_pack = jnp.concatenate([adj_rows[:, :, 0:width], state_rows[:, :, 0:far]], axis=2)
    next_pack = next_pack.at[1, :, far].set(lanes(damp_rows[:, 0:far]))
    prev_pack = jnp.concatenate(
        [adj_rows[:, :, azim_local - width :], state_rows[:, :, azim_local - far :]], axis=2
    )
    prev_pack = prev_pack.at[1, :, 0].set(lanes(damp_rows[:, azim_local - far :]))
    azim_prev = lax.ppermute(prev_pack, "az", [(i, (i + 1) % az_count) for i in range(az_count)])
    azim_next = lax.ppermute(next_pack, "az", [((i + 1) % az_count, i) for i in range(az_count)])

    rows = axial_local + 2 * width
    cols = azim_local + 2 * width
    axis_index = jnp.reshape(lax.axis_index("ax"), (1,)).astype(jnp.int32)
    kernel = functools.partial(
        steps_kernel, axial_local, azim_local, radial_count, width, axial_local * ax_count
    )
    vmem = pl.BlockSpec(memory_space=pltpu.VMEM)
    slot_total = 2 * resistance.shape[0]
    owned = slot_total // az_count
    cell_slot = patch_slot_index[wall_patch].reshape(-1)
    senders = ax_count * az_count
    owner = (cell_slot[None, :] // owned == jnp.arange(senders, dtype=jnp.int32)[:, None] % az_count).astype(jnp.float32)
    place = (cell_slot[:, None] % owned == jnp.arange(owned, dtype=jnp.int32)[None, :]).astype(jnp.float32)
    adjoint, send = pl.pallas_call(
        kernel,
        out_shape=(
            jax.ShapeDtypeStruct(state.shape, jnp.float32),
            jax.ShapeDtypeStruct((senders, owned), jnp.float32),
        ),
        in_specs=[pl.BlockSpec(memory_space=pltpu.SMEM)] + [vmem] * 9,
        out_specs=(vmem, vmem),
        scratch_shapes=[pltpu.VMEM((4, rows, cols, radial_count), jnp.float32)] * 4
        + [
            pltpu.VMEM((rows, cols, radial_count), jnp.float32),
            pltpu.VMEM((ITERS, axial_local, azim_local, radial_count), jnp.float32),
            pltpu.VMEM((ITERS, axial_local, azim_local, radial_count), jnp.float32),
        ],
    )(axis_index, state, final_adjoint, liner, axial_lo, axial_hi, azim_next, azim_prev, owner, place)
    patch_gradient = lax.all_to_all(send, ("ax", "az"), 0, 0, tiled=True).sum(0)
    return (adjoint, patch_gradient)


def solution(mesh):
    return jax.shard_map(
        shards,
        mesh=mesh,
        in_specs=(P(None, "ax", "az", None), P(None, "ax", "az", None), P(), P("ax", "az"), P()),
        out_specs=(P(None, "ax", "az", None), P("az")),
        check_vma=False,
    )
```

```python
import functools

import jax
import jax.numpy as jnp
from jax import lax
from jax.experimental import pallas as pl
from jax.experimental.pallas import tpu as pltpu
from jax.sharding import PartitionSpec as P

ITERS = 4
UNROLL = 6


mach_number = 0.5
time_step = 0.3


def steps_kernel(
    axial_local, azim_local, radial_count, width, axial_total,
    axis_ref, state_ref, adjoint_ref, liner_ref, axial_lo_ref, axial_hi_ref, azim_next_ref, azim_prev_ref,
    owner_ref, place_ref,
    out_ref, send_ref,
    field_a, field_b, adj_a, adj_b, liner_pad, walls, adj_walls,
):
    rows = axial_local + 2 * width
    cols = azim_local + 2 * width
    own = slice(width, width + axial_local)
    own_cols = slice(0, azim_local)

    far = width - 1
    halo_cols = slice(azim_local, cols)
    for buf in (field_a, adj_a):
        buf[:, 0, halo_cols] = jnp.zeros((4, 2 * width, radial_count), jnp.float32)
        buf[:, rows - 1, halo_cols] = jnp.zeros((4, 2 * width, radial_count), jnp.float32)
    field_a[:, :, azim_local + far : azim_local + width + 1] = jnp.zeros((4, rows, 2, radial_count), jnp.float32)
    liner_pad[...] = jnp.zeros(liner_pad.shape, jnp.float32)
    for buf, lo in ((field_a, 0), (adj_a, 4)):
        buf[:, own, own_cols] = state_ref[...] if lo == 0 else adjoint_ref[...]
        buf[:, 0:width, own_cols] = axial_lo_ref[lo : lo + 4]
        buf[:, width + axial_local : rows, own_cols] = axial_hi_ref[lo : lo + 4]
    inner = slice(1, rows - 1)
    adj_a[:, inner, azim_local : azim_local + width] = azim_next_ref[:, :, 0:width]
    adj_a[:, inner, azim_local + width : cols] = azim_prev_ref[:, :, 0:width]
    field_a[:, inner, azim_local : azim_local + far] = azim_next_ref[:, :, width : width + far]
    field_a[:, inner, cols - far : cols] = azim_prev_ref[:, :, width : width + far]
    liner_pad[own, own_cols] = liner_ref[...]
    liner_pad[0:width, own_cols] = axial_lo_ref[8]
    liner_pad[width + axial_local : rows, own_cols] = axial_hi_ref[8]
    strip_lane = lax.broadcasted_iota(jnp.int32, (rows - 2, 1, radial_count), 2)
    next_damp = azim_next_ref[1, :, far : far + 1, :]
    prev_damp = azim_prev_ref[1, :, 0:1, :]
    for m in range(far):
        col = azim_local + m
        liner_pad[inner, col : col + 1] = jnp.where(
            strip_lane == radial_count - 1, pltpu.roll(next_damp, radial_count - 1 - m, 2), 0.0
        )
        col = cols - far + m
        liner_pad[inner, col : col + 1] = jnp.where(
            strip_lane == radial_count - 1, pltpu.roll(prev_damp, radial_count - 1 - m, 2), 0.0
        )

    first_row = axis_ref[0] * axial_local - width
    lane = lax.broadcasted_iota(jnp.int32, (cols, radial_count), 1)
    not_last = lane != radial_count - 1
    not_first = lane != 0

    def radial_diff(x):
        upper = jnp.where(not_last, pltpu.roll(x, radial_count - 1, 1), 0.0)
        lower = jnp.where(not_first, pltpu.roll(x, 1, 1), 0.0)
        return (upper - lower) * 0.5

    def azim_diff(x):
        return (pltpu.roll(x, cols - 1, 0) - pltpu.roll(x, 1, 0)) * 0.5

    def row(src, dst, r, orient, keep):
        centre = src[:, r]
        along = (src[:, r + 1] - src[:, r - 1]) * 0.5
        press, axial, azim, radial = centre[0], centre[1], centre[2], centre[3]
        rate_press = (
            orient * (-mach_number * along[0] - along[1] - azim_diff(azim) - radial_diff(radial))
            - liner_pad[r] * press
        )
        rate_axial = orient * (-mach_number * along[1] - along[0])
        rate_azim = orient * (-mach_number * along[2] - azim_diff(press))
        rate_radial = orient * (-mach_number * along[3] - radial_diff(press))
        dst[0, r] = (press + time_step * rate_press) * keep
        dst[1, r] = (axial + time_step * rate_axial) * keep
        dst[2, r] = (azim + time_step * rate_azim) * keep
        dst[3, r] = (radial + time_step * rate_radial) * keep

    def advance(chains, step):
        def body(r, carry):
            g = first_row + r
            keep = jnp.where((g >= 0) & (g < axial_total), 1.0, 0.0)
            for src, dst, orient in chains:
                row(src, dst, r, orient, keep)
            return carry

        lax.fori_loop(step, rows - step, body, 0, unroll=UNROLL)

    walls[0] = state_ref[0]
    adj_walls[0] = adjoint_ref[0]
    fwd = (field_a, field_b)
    adj = (adj_a, adj_b)
    for step in range(1, ITERS + 1):
        chains = [(adj[(step - 1) % 2], adj[step % 2], -1.0)]
        if step < ITERS:
            chains.append((fwd[(step - 1) % 2], fwd[step % 2], 1.0))
        advance(chains, step)
        if step < ITERS:
            walls[step] = fwd[step % 2][0, own, own_cols]
            adj_walls[step] = adj[step % 2][0, own, own_cols]

    grad = jnp.zeros(walls.shape[1:], jnp.float32)
    for step in range(1, ITERS + 1):
        grad = grad - time_step * adj_walls[step - 1] * walls[ITERS - step]
    by_cell = grad.reshape(axial_local * azim_local, radial_count)
    wall_lane = (lax.broadcasted_iota(jnp.int32, (8, radial_count), 1) == radial_count - 1).astype(jnp.float32)
    cell_row = lax.dot_general(
        wall_lane, by_cell, (((1,), (1,)), ((), ())),
        precision=lax.Precision.HIGHEST, preferred_element_type=jnp.float32,
    )[0:1]
    send_ref[...] = jnp.dot(
        owner_ref[...] * cell_row, place_ref[...],
        precision=lax.Precision.HIGHEST, preferred_element_type=jnp.float32,
    )
    out_ref[...] = adj[ITERS % 2][:, own, own_cols]


def shards(state, final_adjoint, resistance, wall_patch, patch_slot_index):
    width = ITERS
    axial_local = state.shape[1]
    azim_local = state.shape[2]
    radial_count = state.shape[3]
    wall = (jnp.arange(radial_count) == radial_count - 1).astype(jnp.float32)
    patch_count = resistance.shape[0]
    patch_onehot = (wall_patch[:, :, None] == jnp.arange(patch_count, dtype=jnp.int32)).astype(jnp.float32)
    damping = jnp.dot(patch_onehot, resistance, precision=lax.Precision.HIGHEST)
    liner = damping[:, :, None] * wall[None, None, :]

    def pack(sl_axis, start, stop):
        parts = [lax.slice_in_dim(x, start, stop, axis=sl_axis) for x in (state, final_adjoint)]
        parts.append(lax.slice_in_dim(liner, start, stop, axis=sl_axis - 1)[None])
        return jnp.concatenate(parts, axis=0)

    ax_count = lax.axis_size("ax")
    az_count = lax.axis_size("az")
    axial_lo, axial_hi = lax.ppermute(
        pack(1, axial_local - width, axial_local), "ax", [(i, i + 1) for i in range(ax_count - 1)]
    ), lax.ppermute(pack(1, 0, width), "ax", [(i + 1, i) for i in range(ax_count - 1)])

    far = width - 1

    def padded_rows(lo, own_block, hi):
        return jnp.concatenate([lo[:, 1:], own_block, hi[:, :-1]], axis=1)

    state_rows = padded_rows(axial_lo[0:4], state, axial_hi[0:4])
    adj_rows = padded_rows(axial_lo[4:8], final_adjoint, axial_hi[4:8])
    damp_rows = jnp.concatenate(
        [axial_lo[8, 1:, :, radial_count - 1], damping, axial_hi[8, :-1, :, radial_count - 1]], axis=0
    )

    def lanes(x):
        return jnp.pad(x, ((0, 0), (0, radial_count - x.shape[1])))

    next_pack = jnp.concatenate([adj_rows[:, :, 0:width], state_rows[:, :, 0:far]], axis=2)
    next_pack = next_pack.at[1, :, far].set(lanes(damp_rows[:, 0:far]))
    prev_pack = jnp.concatenate(
        [adj_rows[:, :, azim_local - width :], state_rows[:, :, azim_local - far :]], axis=2
    )
    prev_pack = prev_pack.at[1, :, 0].set(lanes(damp_rows[:, azim_local - far :]))
    azim_prev = lax.ppermute(prev_pack, "az", [(i, (i + 1) % az_count) for i in range(az_count)])
    azim_next = lax.ppermute(next_pack, "az", [((i + 1) % az_count, i) for i in range(az_count)])

    rows = axial_local + 2 * width
    cols = azim_local + 2 * width
    axis_index = jnp.reshape(lax.axis_index("ax"), (1,)).astype(jnp.int32)
    kernel = functools.partial(
        steps_kernel, axial_local, azim_local, radial_count, width, axial_local * ax_count
    )
    vmem = pl.BlockSpec(memory_space=pltpu.VMEM)
    slot_total = 2 * resistance.shape[0]
    owned = slot_total // az_count
    cell_slot = patch_slot_index[wall_patch].reshape(-1)
    senders = ax_count * az_count
    owner = (cell_slot[None, :] // owned == jnp.arange(senders, dtype=jnp.int32)[:, None] % az_count).astype(jnp.float32)
    place = (cell_slot[:, None] % owned == jnp.arange(owned, dtype=jnp.int32)[None, :]).astype(jnp.float32)
    adjoint, send = pl.pallas_call(
        kernel,
        out_shape=(
            jax.ShapeDtypeStruct(state.shape, jnp.float32),
            jax.ShapeDtypeStruct((senders, owned), jnp.float32),
        ),
        in_specs=[pl.BlockSpec(memory_space=pltpu.SMEM)] + [vmem] * 9,
        out_specs=(vmem, vmem),
        scratch_shapes=[pltpu.VMEM((4, rows, cols, radial_count), jnp.float32)] * 4
        + [
            pltpu.VMEM((rows, cols, radial_count), jnp.float32),
            pltpu.VMEM((ITERS, axial_local, azim_local, radial_count), jnp.float32),
            pltpu.VMEM((ITERS, axial_local, azim_local, radial_count), jnp.float32),
        ],
    )(axis_index, state, final_adjoint, liner, axial_lo, axial_hi, azim_next, azim_prev, owner, place)
    patch_gradient = lax.all_to_all(send, ("ax", "az"), 0, 0, tiled=True).sum(0)
    return (adjoint, patch_gradient)


def solution(mesh):
    return jax.shard_map(
        shards,
        mesh=mesh,
        in_specs=(P(None, "ax", "az", None), P(None, "ax", "az", None), P(), P("ax", "az"), P()),
        out_specs=(P(None, "ax", "az", None), P("az")),
        check_vma=False,
    )
```

```python
import functools

import jax
import jax.numpy as jnp
from jax import lax
from jax.experimental import pallas as pl
from jax.experimental.pallas import tpu as pltpu
from jax.sharding import PartitionSpec as P

ITERS = 4
UNROLL = 6


mach_number = 0.5
time_step = 0.3


def steps_kernel(
    axial_local, azim_local, radial_count, width, axial_total,
    axis_ref, state_ref, adjoint_ref, liner_ref, axial_lo_ref, axial_hi_ref, azim_next_ref, azim_prev_ref,
    owner_ref, place_ref,
    out_ref, send_ref,
    field_a, field_b, adj_a, adj_b, liner_pad, walls, adj_walls,
):
    rows = axial_local + 2 * width
    cols = azim_local + 2 * width
    own = slice(width, width + axial_local)
    own_cols = slice(0, azim_local)

    far = width - 1
    halo_cols = slice(azim_local, cols)
    for buf in (field_a, adj_a):
        buf[:, 0, halo_cols] = jnp.zeros((4, 2 * width, radial_count), jnp.float32)
        buf[:, rows - 1, halo_cols] = jnp.zeros((4, 2 * width, radial_count), jnp.float32)
    field_a[:, :, azim_local + far : azim_local + width + 1] = jnp.zeros((4, rows, 2, radial_count), jnp.float32)
    liner_pad[...] = jnp.zeros(liner_pad.shape, jnp.float32)
    for buf, lo in ((field_a, 0), (adj_a, 4)):
        buf[:, own, own_cols] = state_ref[...] if lo == 0 else adjoint_ref[...]
        buf[:, 0:width, own_cols] = axial_lo_ref[lo : lo + 4]
        buf[:, width + axial_local : rows, own_cols] = axial_hi_ref[lo : lo + 4]
    inner = slice(1, rows - 1)
    adj_a[:, inner, azim_local : azim_local + width] = azim_next_ref[:, :, 0:width]
    adj_a[:, inner, azim_local + width : cols] = azim_prev_ref[:, :, 0:width]
    field_a[:, inner, azim_local : azim_local + far] = azim_next_ref[:, :, width : width + far]
    field_a[:, inner, cols - far : cols] = azim_prev_ref[:, :, width : width + far]
    liner_pad[own, own_cols] = liner_ref[...]
    liner_pad[0:width, own_cols] = axial_lo_ref[8]
    liner_pad[width + axial_local : rows, own_cols] = axial_hi_ref[8]
    strip_lane = lax.broadcasted_iota(jnp.int32, (rows - 2, 1, radial_count), 2)
    next_damp = azim_next_ref[1, :, far : far + 1, :]
    prev_damp = azim_prev_ref[1, :, 0:1, :]
    for m in range(far):
        col = azim_local + m
        liner_pad[inner, col : col + 1] = jnp.where(
            strip_lane == radial_count - 1, pltpu.roll(next_damp, radial_count - 1 - m, 2), 0.0
        )
        col = cols - far + m
        liner_pad[inner, col : col + 1] = jnp.where(
            strip_lane == radial_count - 1, pltpu.roll(prev_damp, radial_count - 1 - m, 2), 0.0
        )

    first_row = axis_ref[0] * axial_local - width
    lane = lax.broadcasted_iota(jnp.int32, (cols, radial_count), 1)
    not_last = lane != radial_count - 1
    not_first = lane != 0

    def radial_diff(x):
        upper = jnp.where(not_last, pltpu.roll(x, radial_count - 1, 1), 0.0)
        lower = jnp.where(not_first, pltpu.roll(x, 1, 1), 0.0)
        return (upper - lower) * 0.5

    def azim_diff(x):
        return (pltpu.roll(x, cols - 1, 0) - pltpu.roll(x, 1, 0)) * 0.5

    def row(src, dst, r, orient, keep):
        centre = src[:, r]
        along = (src[:, r + 1] - src[:, r - 1]) * 0.5
        press, axial, azim, radial = centre[0], centre[1], centre[2], centre[3]
        rate_press = (
            orient * (-mach_number * along[0] - along[1] - azim_diff(azim) - radial_diff(radial))
            - liner_pad[r] * press
        )
        rate_axial = orient * (-mach_number * along[1] - along[0])
        rate_azim = orient * (-mach_number * along[2] - azim_diff(press))
        rate_radial = orient * (-mach_number * along[3] - radial_diff(press))
        dst[0, r] = (press + time_step * rate_press) * keep
        dst[1, r] = (axial + time_step * rate_axial) * keep
        dst[2, r] = (azim + time_step * rate_azim) * keep
        dst[3, r] = (radial + time_step * rate_radial) * keep

    def advance(chains, step):
        def body(r, carry):
            g = first_row + r
            keep = jnp.where((g >= 0) & (g < axial_total), 1.0, 0.0)
            for src, dst, orient in chains:
                row(src, dst, r, orient, keep)
            return carry

        lax.fori_loop(step, rows - step, body, 0, unroll=UNROLL)

    walls[0] = state_ref[0]
    adj_walls[0] = adjoint_ref[0]
    fwd = (field_a, field_b)
    adj = (adj_a, adj_b)
    for step in range(1, ITERS + 1):
        chains = [(adj[(step - 1) % 2], adj[step % 2], -1.0)]
        if step < ITERS:
            chains.append((fwd[(step - 1) % 2], fwd[step % 2], 1.0))
        advance(chains, step)
        if step < ITERS:
            walls[step] = fwd[step % 2][0, own, own_cols]
            adj_walls[step] = adj[step % 2][0, own, own_cols]

    grad = jnp.zeros(walls.shape[1:], jnp.float32)
    for step in range(1, ITERS + 1):
        grad = grad - time_step * adj_walls[step - 1] * walls[ITERS - step]
    by_cell = grad.reshape(axial_local * azim_local, radial_count)
    wall_lane = (lax.broadcasted_iota(jnp.int32, (8, radial_count), 1) == radial_count - 1).astype(jnp.float32)
    cell_row = lax.dot_general(
        wall_lane, by_cell, (((1,), (1,)), ((), ())),
        precision=lax.Precision.HIGHEST, preferred_element_type=jnp.float32,
    )[0:1]
    send_ref[...] = jnp.dot(
        owner_ref[...] * cell_row, place_ref[...],
        precision=lax.Precision.HIGHEST, preferred_element_type=jnp.float32,
    )
    out_ref[...] = adj[ITERS % 2][:, own, own_cols]


def shards(state, final_adjoint, resistance, wall_patch, patch_slot_index):
    width = ITERS
    axial_local = state.shape[1]
    azim_local = state.shape[2]
    radial_count = state.shape[3]
    wall = (jnp.arange(radial_count) == radial_count - 1).astype(jnp.float32)
    patch_count = resistance.shape[0]
    high = lax.reduce_precision(resistance, exponent_bits=8, mantissa_bits=7)
    rest = resistance - high
    middle = lax.reduce_precision(rest, exponent_bits=8, mantissa_bits=7)
    low = rest - middle
    table = jnp.stack([high, middle, low], axis=1).astype(jnp.bfloat16)
    patch_onehot = (wall_patch[:, :, None] == jnp.arange(patch_count, dtype=jnp.int32)).astype(jnp.bfloat16)
    parts = jnp.dot(patch_onehot, table, preferred_element_type=jnp.float32)
    damping = (parts[..., 0] + parts[..., 1]) + parts[..., 2]
    liner = damping[:, :, None] * wall[None, None, :]

    def pack(sl_axis, start, stop):
        parts = [lax.slice_in_dim(x, start, stop, axis=sl_axis) for x in (state, final_adjoint)]
        parts.append(lax.slice_in_dim(liner, start, stop, axis=sl_axis - 1)[None])
        return jnp.concatenate(parts, axis=0)

    ax_count = lax.axis_size("ax")
    az_count = lax.axis_size("az")
    axial_lo, axial_hi = lax.ppermute(
        pack(1, axial_local - width, axial_local), "ax", [(i, i + 1) for i in range(ax_count - 1)]
    ), lax.ppermute(pack(1, 0, width), "ax", [(i + 1, i) for i in range(ax_count - 1)])

    far = width - 1

    def padded_rows(lo, own_block, hi):
        return jnp.concatenate([lo[:, 1:], own_block, hi[:, :-1]], axis=1)

    state_rows = padded_rows(axial_lo[0:4], state, axial_hi[0:4])
    adj_rows = padded_rows(axial_lo[4:8], final_adjoint, axial_hi[4:8])
    damp_rows = jnp.concatenate(
        [axial_lo[8, 1:, :, radial_count - 1], damping, axial_hi[8, :-1, :, radial_count - 1]], axis=0
    )

    def lanes(x):
        return jnp.pad(x, ((0, 0), (0, radial_count - x.shape[1])))

    next_pack = jnp.concatenate([adj_rows[:, :, 0:width], state_rows[:, :, 0:far]], axis=2)
    next_pack = next_pack.at[1, :, far].set(lanes(damp_rows[:, 0:far]))
    prev_pack = jnp.concatenate(
        [adj_rows[:, :, azim_local - width :], state_rows[:, :, azim_local - far :]], axis=2
    )
    prev_pack = prev_pack.at[1, :, 0].set(lanes(damp_rows[:, azim_local - far :]))
    azim_prev = lax.ppermute(prev_pack, "az", [(i, (i + 1) % az_count) for i in range(az_count)])
    azim_next = lax.ppermute(next_pack, "az", [((i + 1) % az_count, i) for i in range(az_count)])

    rows = axial_local + 2 * width
    cols = azim_local + 2 * width
    axis_index = jnp.reshape(lax.axis_index("ax"), (1,)).astype(jnp.int32)
    kernel = functools.partial(
        steps_kernel, axial_local, azim_local, radial_count, width, axial_local * ax_count
    )
    vmem = pl.BlockSpec(memory_space=pltpu.VMEM)
    slot_total = 2 * resistance.shape[0]
    owned = slot_total // az_count
    cell_slot = patch_slot_index[wall_patch].reshape(-1)
    senders = ax_count * az_count
    owner = (cell_slot[None, :] // owned == jnp.arange(senders, dtype=jnp.int32)[:, None] % az_count).astype(jnp.float32)
    place = (cell_slot[:, None] % owned == jnp.arange(owned, dtype=jnp.int32)[None, :]).astype(jnp.float32)
    adjoint, send = pl.pallas_call(
        kernel,
        out_shape=(
            jax.ShapeDtypeStruct(state.shape, jnp.float32),
            jax.ShapeDtypeStruct((senders, owned), jnp.float32),
        ),
        in_specs=[pl.BlockSpec(memory_space=pltpu.SMEM)] + [vmem] * 9,
        out_specs=(vmem, vmem),
        scratch_shapes=[pltpu.VMEM((4, rows, cols, radial_count), jnp.float32)] * 4
        + [
            pltpu.VMEM((rows, cols, radial_count), jnp.float32),
            pltpu.VMEM((ITERS, axial_local, azim_local, radial_count), jnp.float32),
            pltpu.VMEM((ITERS, axial_local, azim_local, radial_count), jnp.float32),
        ],
    )(axis_index, state, final_adjoint, liner, axial_lo, axial_hi, azim_next, azim_prev, owner, place)
    patch_gradient = lax.all_to_all(send, ("ax", "az"), 0, 0, tiled=True).sum(0)
    return (adjoint, patch_gradient)


def solution(mesh):
    return jax.shard_map(
        shards,
        mesh=mesh,
        in_specs=(P(None, "ax", "az", None), P(None, "ax", "az", None), P(), P("ax", "az"), P()),
        out_specs=(P(None, "ax", "az", None), P("az")),
        check_vma=False,
    )
```
